256 devices in a mesh: section: 4 (over y_lo, core), dp: 64 (over y_hi, z, x).
Axes of the slice: x: 4, y: 4 (y_hi: 2, y_lo: 2; y = y_hi * 2 + y_lo), z: 8, core: 2. Of those that a mesh axis runs over, the one named last changes fastest.
Arguments:
- token_states: bfloat16 [4, 1024, 8192], P(None, 'dp'), may hold values from -10 to 10
- norm_gains: float32 [4, 8192], P('section'), may hold values from 1 to 4
- prompt_kv: bfloat16 [4, 1024, 2048], P('section'), may hold values from -11 to 11
- history_kv: bfloat16 [4, 1024, 28, 2048], P('section', 'dp'), may hold values from -6 to 6
- new_kv: bfloat16 [4, 4, 1024, 2048], P('section', None, 'dp'), may hold values from -6 to 6
- ancestors: int32 [1024], replicated, may hold values from 0 to 1023, as said below
Outputs:
- attention_out: bfloat16 [4, 4, 1024, 8192], P('section', None, 'dp')
- forked_kv: bfloat16 [4, 1024, 32, 2048], P('section', 'dp')
The draws below stay inside these ranges and needn't reach their ends.
Inputs may be any that keep to these rules, and one draw needn't show every extreme that they name: Of the 16 ancestors of particles p * 16 .. p * 16 + 15, at most one distinct value lies in any block q * 16 .. q * 16 + 15; ancestors may repeat.
All inputs are finite; a program needn't handle non-finite values.
Results may differ from the reference program's by a relative error of at most 0.0086.
Values may be sent and summed in bfloat16 or wider, within the bound.
No kernel may reach another device: no remote copies, remote signals or barrier semaphores. Data moves between devices by JAX's collectives and lax.ppermute only.
A program may use at most 128 MiB of HBM per device.

```python
import math
import jax
import jax.numpy as jnp
from jax import lax

D = 8192
HEADS = 64
KV_HEADS = 8
HEAD_DIM = 128
KVW = 2048
STEPS = 4
PROMPT = 1024
HIST = 28
PART_DEV = 16
LAYERS = 4
PARTICLES = 1024


def draw_ancestors(key, part):
    shard_count = PARTICLES // PART_DEV
    chosen = min(PART_DEV // 2, shard_count)

    def one_shard(index):
        inner = jax.random.fold_in(jax.random.fold_in(key, 7919), index)
        shard_key, pick_key, extra_key, order_key = jax.random.split(inner, 4)
        sources = jax.random.permutation(shard_key, shard_count)[:chosen]
        within = jax.random.randint(pick_key, (chosen,), 0, PART_DEV)
        distinct = sources * PART_DEV + within
        repeats = jax.random.randint(extra_key, (PART_DEV - chosen,), 0, chosen)
        slots = jnp.concatenate([distinct, distinct[repeats]])
        order = jax.random.permutation(order_key, PART_DEV)
        return slots[order]
    table = jax.vmap(one_shard)(jnp.arange(shard_count))
    return table.reshape(PARTICLES).astype(jnp.int32)


def draw_token_states(key, part):
    jitter_key = jax.random.fold_in(jax.random.fold_in(key, 11), 0)
    array_shape = (STEPS, PARTICLES, D)
    return jnp.clip(jax.random.normal(jitter_key, array_shape, jnp.float32), -6.0, 6.0).astype(jnp.bfloat16)


def draw_norm_gains(key, part):
    spread = jax.random.uniform(jax.random.fold_in(key, 23), (LAYERS, D), jnp.float32, 0.0, math.log(4.0))
    return jnp.exp(spread)


def draw_prompt_kv(key, part):
    base_key = jax.random.fold_in(jax.random.fold_in(key, 31), 0)
    array_shape = (LAYERS, PROMPT, KVW)
    return jnp.clip(jax.random.normal(base_key, array_shape, jnp.float32), -6.0, 6.0).astype(jnp.bfloat16)


def steps_of(stream_key, shape, cuts, least, largest):
    gain = 1.0
    for axis_at, blocks in cuts:
        steps = jax.random.uniform(jax.random.fold_in(jax.random.fold_in(stream_key, 6), axis_at), (blocks,), jnp.float32, least / len(cuts), largest / len(cuts))
        gain = gain * jnp.repeat(jnp.exp(steps), shape[axis_at] // blocks).reshape((-1,) + (1,) * (len(shape) - 1 - axis_at))
    return gain


def noise(stream_key, shape, scale, bound, cuts=(), held_as=jnp.bfloat16):
    level = steps_of(stream_key, shape, cuts, -0.22, 0.18) if cuts else 1.0
    drawn = jax.random.normal(stream_key, shape, jnp.float32) * scale * level
    return jnp.minimum(jnp.maximum(drawn, -bound), bound).astype(held_as)


def setup_inputs(seed: int = 0) -> dict:
    key_of = jax.random.split(jax.random.key(seed), 7)
    token_states = draw_token_states(jax.random.fold_in(key_of[6], 71), 0)
    norm_gains = draw_norm_gains(jax.random.fold_in(key_of[6], 71), 0)
    prompt_kv = draw_prompt_kv(jax.random.fold_in(key_of[6], 71), 0)
    history_kv = noise(key_of[3], (LAYERS, PARTICLES, HIST, KVW), 1.0, 6.0, ((0, 4), (1, 64)))
    new_kv = noise(key_of[4], (LAYERS, STEPS, PARTICLES, KVW), 1.0, 6.0, ((0, 4), (2, 64)))
    ancestors = draw_ancestors(jax.random.fold_in(key_of[6], 71), 0)
    return dict(token_states=token_states, norm_gains=norm_gains, prompt_kv=prompt_kv, history_kv=history_kv, new_kv=new_kv, ancestors=ancestors)


NEG_FILL = -1e+30

def normalize(values):
    return values * lax.rsqrt(lax.optimization_barrier(jnp.mean(values * values, axis=-1, keepdims=True)) + 1e-05)

def attend(hidden, gains_row, prompt, history, recent, step_now):
    rows = hidden.shape[0]
    half = KV_HEADS * HEAD_DIM
    share = HEADS // KV_HEADS
    rounded = (normalize(hidden) * gains_row).astype(jnp.bfloat16)
    queries = lax.optimization_barrier(rounded).astype(jnp.float32).reshape(rows, KV_HEADS, share, HEAD_DIM)
    prompt_keys = prompt[:, :half].astype(jnp.float32).reshape(-1, KV_HEADS, HEAD_DIM)
    prompt_vals = prompt[:, half:].astype(jnp.float32).reshape(-1, KV_HEADS, HEAD_DIM)
    past_keys = history[..., :half].astype(jnp.float32).reshape(rows, -1, KV_HEADS, HEAD_DIM)
    past_vals = history[..., half:].astype(jnp.float32).reshape(rows, -1, KV_HEADS, HEAD_DIM)
    recent_keys = recent[..., :half].astype(jnp.float32).reshape(-1, rows, KV_HEADS, HEAD_DIM)
    recent_vals = recent[..., half:].astype(jnp.float32).reshape(-1, rows, KV_HEADS, HEAD_DIM)
    score_scale = HEAD_DIM ** (-0.5)
    prompt_scores = jnp.einsum('pkgd,nkd->pkgn', queries, prompt_keys) * score_scale
    past_scores = jnp.einsum('pkgd,pnkd->pkgn', queries, past_keys) * score_scale
    recent_scores = jnp.einsum('pkgd,npkd->pkgn', queries, recent_keys) * score_scale
    present = jnp.arange(recent.shape[0]) <= step_now
    recent_scores = jnp.where(present, recent_scores, NEG_FILL)
    highest = jnp.maximum(lax.optimization_barrier(jnp.max(prompt_scores, -1, keepdims=True)), lax.optimization_barrier(jnp.max(past_scores, -1, keepdims=True)))
    highest = jnp.maximum(highest, lax.optimization_barrier(jnp.max(recent_scores, -1, keepdims=True)))
    prompt_exp = jnp.exp(prompt_scores - highest)
    past_exp = jnp.exp(past_scores - highest)
    recent_exp = jnp.exp(recent_scores - highest)
    denominator = lax.optimization_barrier(jnp.sum(prompt_exp, -1, keepdims=True)) + lax.optimization_barrier(jnp.sum(past_exp, -1, keepdims=True)) + lax.optimization_barrier(jnp.sum(recent_exp, -1, keepdims=True))

    def weigh(portion):
        return lax.optimization_barrier((portion / denominator).astype(jnp.bfloat16)).astype(jnp.float32)
    mixed = jnp.einsum('pkgn,nkd->pkgd', weigh(prompt_exp), prompt_vals)
    mixed = mixed + jnp.einsum('pkgn,pnkd->pkgd', weigh(past_exp), past_vals)
    mixed = mixed + jnp.einsum('pkgn,npkd->pkgd', weigh(recent_exp), recent_vals)
    return mixed.reshape(rows, HEADS * HEAD_DIM)

def reference(token_states, norm_gains, prompt_kv, history_kv, new_kv, ancestors):
    layer_count = norm_gains.shape[0]
    results = [[None] * STEPS for layer in range(layer_count)]
    previous = None
    for step in range(STEPS):
        residual = token_states[step].astype(jnp.float32)
        if step > 0:
            residual = residual + normalize(previous)
        for layer in range(layer_count):
            mixed = attend(residual, norm_gains[layer], prompt_kv[layer], history_kv[layer], new_kv[layer], step)
            results[layer][step] = mixed.astype(jnp.bfloat16)
            residual = residual + mixed
        previous = residual
    attention_out = jnp.stack([jnp.stack(results[layer], 0) for layer in range(layer_count)], 0)
    particle_cache = jnp.concatenate([history_kv, jnp.transpose(new_kv, (0, 2, 1, 3))], axis=2)
    forked_kv = jnp.take(particle_cache, ancestors.astype(jnp.int32), axis=1)
    return (attention_out, forked_kv)
```

```python
import jax
import jax.numpy as jnp
from jax import lax
from jax.experimental import pallas as pl
from jax.experimental.pallas import tpu as pltpu
from jax.sharding import PartitionSpec as P


HEADS = 64
KV_HEADS = 8
HEAD_DIM = 128


NEG_FILL = -1e30


def passed_along(block, axis, distance):
    devices = range(lax.axis_size(axis))
    route = [((i - distance) % len(devices), i) for i in devices]
    return lax.ppermute(block, axis, route)


def normalize(values):
    return values * lax.rsqrt(jnp.mean(values * values, axis=-1, keepdims=True) + 1e-05)


HEAD_BLOCK = 2
INTERPRET = False


def stage_kernel(tokens, hist, head_block):
    score_scale = HEAD_DIM ** (-0.5)

    def kernel(sc_ref, q_ref, pk_ref, pv_ref, ck_ref, cv_ref, o_ref):
        step_now = sc_ref[0]
        rows = q_ref.shape[1]
        width = ck_ref.shape[0]
        row_id = lax.broadcasted_iota(jnp.int32, (rows, width), 0)
        col_id = lax.broadcasted_iota(jnp.int32, (rows, width), 1)
        share = HEADS // KV_HEADS
        valid = (row_id // share == col_id // tokens) & (col_id % tokens < hist + 1 + step_now)
        for h in range(head_block):
            cols = slice(h * HEAD_DIM, (h + 1) * HEAD_DIM)
            q = q_ref[h]
            dims = (((1,), (1,)), ((), ()))
            prompt_scores = (
                lax.dot_general(q, pk_ref[:, cols], dims, preferred_element_type=jnp.float32)
                * score_scale
            )
            cache_scores = (
                lax.dot_general(q, ck_ref[:, cols], dims, preferred_element_type=jnp.float32)
                * score_scale
            )
            cache_scores = jnp.where(valid, cache_scores, NEG_FILL)
            highest = jnp.maximum(
                jnp.max(prompt_scores, -1, keepdims=True), jnp.max(cache_scores, -1, keepdims=True)
            )
            prompt_exp = jnp.exp(prompt_scores - highest)
            cache_exp = jnp.exp(cache_scores - highest)
            denominator = jnp.sum(prompt_exp, -1, keepdims=True) + jnp.sum(
                cache_exp, -1, keepdims=True
            )
            mixed = jnp.dot(
                (prompt_exp / denominator).astype(jnp.bfloat16),
                pv_ref[:, cols],
                preferred_element_type=jnp.float32,
            )
            mixed = mixed + jnp.dot(
                (cache_exp / denominator).astype(jnp.bfloat16),
                cv_ref[:, cols],
                preferred_element_type=jnp.float32,
            )
            o_ref[h] = mixed

    return kernel


def attend(hidden, gains_row, prompt, cache, step_now, group_now, hist_len, tokens):
    rows = hidden.shape[0]
    share = HEADS // KV_HEADS
    queries = (
        (normalize(hidden) * gains_row)
        .astype(jnp.bfloat16)
        .reshape(rows, KV_HEADS, share, HEAD_DIM)
        .transpose(1, 0, 2, 3)
        .reshape(KV_HEADS, rows * share, HEAD_DIM)
    )
    hb = HEAD_BLOCK
    nb = KV_HEADS // hb
    width = hb * HEAD_DIM
    scalars = jnp.stack([step_now, group_now]).astype(jnp.int32)
    grid_spec = pltpu.PrefetchScalarGridSpec(
        num_scalar_prefetch=1,
        grid=(nb,),
        in_specs=[
            pl.BlockSpec((hb, rows * share, HEAD_DIM), lambda i, sc: (i, 0, 0)),
            pl.BlockSpec((prompt.shape[0], width), lambda i, sc: (0, i)),
            pl.BlockSpec((prompt.shape[0], width), lambda i, sc: (0, i + nb)),
            pl.BlockSpec((rows * tokens, width), lambda i, sc: (sc[1], i)),
            pl.BlockSpec((rows * tokens, width), lambda i, sc: (sc[1], i + nb)),
        ],
        out_specs=pl.BlockSpec((hb, rows * share, HEAD_DIM), lambda i, sc: (i, 0, 0)),
    )
    mixed = pl.pallas_call(
        stage_kernel(tokens, hist_len, hb),
        grid_spec=grid_spec,
        out_shape=jax.ShapeDtypeStruct((KV_HEADS, rows * share, HEAD_DIM), jnp.float32),
        compiler_params=pltpu.CompilerParams(dimension_semantics=("arbitrary",)),
        interpret=INTERPRET,
    )(scalars, queries, prompt, prompt, cache, cache)
    return (
        mixed.reshape(KV_HEADS, rows, share, HEAD_DIM)
        .transpose(1, 0, 2, 3)
        .reshape(rows, HEADS * HEAD_DIM)
    )


def fork_cache(history, recent, ancestors, part_dev):
    shards = lax.axis_size("dp")
    own_index = lax.axis_index("dp")
    particle_cache = jnp.concatenate([history, jnp.transpose(recent, (1, 0, 2))], axis=1)
    owners = ancestors.reshape(shards, part_dev)
    picked = jnp.max(jnp.where(owners // part_dev == own_index, owners % part_dev, 0), axis=1)
    outgoing = jnp.take(particle_cache, picked, axis=0)
    incoming = lax.all_to_all(outgoing, "dp", split_axis=0, concat_axis=0, tiled=True)
    own_ancestors = lax.dynamic_slice_in_dim(ancestors, own_index * part_dev, part_dev)
    return jnp.take(incoming, own_ancestors // part_dev, axis=0)[None]


def local(token_states, norm_gains, prompt_kv, history_kv, new_kv, ancestors):
    section_count = lax.axis_size("section")
    section_index = lax.axis_index("section")
    part_dev = history_kv.shape[1]
    steps = new_kv.shape[1]
    model_width = token_states.shape[2]
    gains_row = norm_gains[0]
    prompt = prompt_kv[0]
    history = history_kv[0]
    recent = new_kv[0]
    cache = jnp.concatenate([history, jnp.transpose(recent, (1, 0, 2))], axis=1).reshape(
        -1, history.shape[2]
    )
    groups = 4
    group_rows = part_dev // groups
    moments = steps * section_count + groups - 1

    def advance(moment, carry):
        arrived, outbuf = carry
        offset = moment - section_index
        step_raw = jnp.floor_divide(offset, section_count)
        group_raw = jnp.mod(offset, section_count)
        active = (offset >= 0) & (step_raw < steps) & (group_raw < groups)
        step_now = jnp.clip(step_raw, 0, steps - 1)
        group_now = jnp.clip(group_raw, 0, groups - 1)
        start = group_now * group_rows
        zero = jnp.zeros((), jnp.int32)
        token_rows = lax.dynamic_slice(
            token_states, (step_now, start, zero), (1, group_rows, model_width)
        )[0].astype(jnp.float32)
        carried = jnp.where(step_now > 0, normalize(arrived), 0.0)
        hidden = jnp.where(section_index == 0, token_rows + carried, arrived)
        mixed = attend(
            hidden, gains_row, prompt, cache, step_now, group_now, history.shape[1], history.shape[1] + steps
        )
        previous = lax.dynamic_slice(outbuf, (step_now, start, zero), (1, group_rows, model_width))
        written = jnp.where(active, mixed.astype(jnp.bfloat16)[None], previous)
        outbuf = lax.dynamic_update_slice(outbuf, written, (step_now, start, zero))
        passed = passed_along(hidden + mixed, "section", 1)
        return (passed, outbuf)

    start_carry = (
        jnp.zeros((group_rows, model_width), jnp.float32),
        jnp.zeros((steps, part_dev, model_width), jnp.bfloat16),
    )
    forked_kv = fork_cache(history, recent, ancestors, part_dev)
    _, outbuf = lax.fori_loop(0, moments, advance, start_carry)
    return (outbuf[None], forked_kv)


def solution(mesh):
    in_specs = (
        P(None, "dp", None),
        P("section", None),
        P("section", None, None),
        P("section", "dp", None, None),
        P("section", None, "dp", None),
        P(),
    )
    out_specs = (P("section", None, "dp", None), P("section", "dp", None, None))
    return jax.shard_map(local, mesh=mesh, in_specs=in_specs, out_specs=out_specs, check_vma=False)
```

```python
import jax
import jax.numpy as jnp
from jax import lax
from jax.experimental import pallas as pl
from jax.experimental.pallas import tpu as pltpu
from jax.sharding import PartitionSpec as P


HEADS = 64
KV_HEADS = 8
HEAD_DIM = 128


NEG_FILL = -1e30


def passed_along(block, axis, distance):
    devices = range(lax.axis_size(axis))
    route = [((i - distance) % len(devices), i) for i in devices]
    return lax.ppermute(block, axis, route)


def normalize(values):
    return values * lax.rsqrt(jnp.mean(values * values, axis=-1, keepdims=True) + 1e-05)


HEAD_BLOCK = 2
INTERPRET = False


def stage_kernel(rows, tokens, hist, head_block):
    score_scale = HEAD_DIM ** (-0.5)
    share = HEADS // KV_HEADS
    group_width = share * HEAD_DIM

    def kernel(
        sc_ref, arr_ref, tok_ref, gain_ref, pk_ref, pv_ref, ck_ref, cv_ref,
        res_ref, att_ref, hid_ref, q_ref,
    ):
        block = pl.program_id(0)

        @pl.when(block == 0)
        def _():
            arrived = arr_ref[...]
            carried = jnp.where(sc_ref[3] > 0, normalize(arrived), 0.0)
            hidden = jnp.where(sc_ref[2] > 0, tok_ref[...].astype(jnp.float32) + carried, arrived)
            queries = (normalize(hidden) * gain_ref[...]).astype(jnp.float32)
            for k in range(KV_HEADS):
                cols = slice(k * group_width, (k + 1) * group_width)
                hid_ref[k] = hidden[:, cols]
                q_ref[k] = queries[:, cols].reshape(rows * share, HEAD_DIM)

        step_now = sc_ref[0]
        width = ck_ref.shape[1]
        row_id = lax.broadcasted_iota(jnp.int32, (rows * share, width), 0)
        col_id = lax.broadcasted_iota(jnp.int32, (rows * share, width), 1)
        valid = (row_id // share == col_id // tokens) & (col_id % tokens < hist + 1 + step_now)
        for h in range(head_block):
            head = block * head_block + h
            cols = slice(h * HEAD_DIM, (h + 1) * HEAD_DIM)
            q = q_ref[head].astype(jnp.bfloat16)
            prompt_scores = (
                jnp.dot(q, pk_ref[cols, :], preferred_element_type=jnp.float32) * score_scale
            )
            cache_scores = (
                jnp.dot(q, ck_ref[cols, :], preferred_element_type=jnp.float32) * score_scale
            )
            cache_scores = jnp.where(valid, cache_scores, NEG_FILL)
            highest = jnp.maximum(
                jnp.max(prompt_scores, -1, keepdims=True), jnp.max(cache_scores, -1, keepdims=True)
            )
            prompt_exp = jnp.exp(prompt_scores - highest)
            cache_exp = jnp.exp(cache_scores - highest)
            denominator = jnp.sum(prompt_exp, -1, keepdims=True) + jnp.sum(
                cache_exp, -1, keepdims=True
            )
            mixed = jnp.dot(
                (prompt_exp / denominator).astype(jnp.bfloat16),
                pv_ref[:, cols],
                preferred_element_type=jnp.float32,
            )
            mixed = mixed + jnp.dot(
                (cache_exp / denominator).astype(jnp.bfloat16),
                cv_ref[:, cols],
                preferred_element_type=jnp.float32,
            )
            mixed = mixed.reshape(rows, group_width)
            out_cols = slice(h * group_width, (h + 1) * group_width)
            res_ref[:, out_cols] = hid_ref[head] + mixed
            att_ref[:, out_cols] = mixed.astype(jnp.bfloat16)

    return kernel


def stage(scalars, arrived, grouped_tokens, gains, prompt_keys_t, prompt, cache_keys_t, cache, hist_len):
    rows, model_width = arrived.shape
    share = HEADS // KV_HEADS
    tokens = cache.shape[0] // (grouped_tokens.shape[1] * rows)
    hb = HEAD_BLOCK
    nb = KV_HEADS // hb
    width = hb * HEAD_DIM
    grid_spec = pltpu.PrefetchScalarGridSpec(
        num_scalar_prefetch=1,
        grid=(nb,),
        in_specs=[
            pl.BlockSpec((rows, model_width), lambda i, sc: (0, 0)),
            pl.BlockSpec((None, None, rows, model_width), lambda i, sc: (sc[0], sc[1], 0, 0)),
            pl.BlockSpec((1, model_width), lambda i, sc: (0, 0)),
            pl.BlockSpec((width, prompt_keys_t.shape[1]), lambda i, sc: (i, 0)),
            pl.BlockSpec((prompt.shape[0], width), lambda i, sc: (0, i + nb)),
            pl.BlockSpec((width, rows * tokens), lambda i, sc: (i, sc[1])),
            pl.BlockSpec((rows * tokens, width), lambda i, sc: (sc[1], i + nb)),
        ],
        out_specs=[
            pl.BlockSpec((rows, hb * share * HEAD_DIM), lambda i, sc: (0, i)),
            pl.BlockSpec((rows, hb * share * HEAD_DIM), lambda i, sc: (0, i)),
        ],
        scratch_shapes=[
            pltpu.VMEM((KV_HEADS, rows, share * HEAD_DIM), jnp.float32),
            pltpu.VMEM((KV_HEADS, rows * share, HEAD_DIM), jnp.float32),
        ],
    )
    return pl.pallas_call(
        stage_kernel(rows, tokens, hist_len, hb),
        grid_spec=grid_spec,
        out_shape=[
            jax.ShapeDtypeStruct((rows, model_width), jnp.float32),
            jax.ShapeDtypeStruct((rows, model_width), jnp.bfloat16),
        ],
        compiler_params=pltpu.CompilerParams(dimension_semantics=("arbitrary",)),
        interpret=INTERPRET,
    )(scalars, arrived, grouped_tokens, gains, prompt_keys_t, prompt, cache_keys_t, cache)


def fork_cache(history, recent, ancestors, part_dev):
    shards = lax.axis_size("dp")
    own_index = lax.axis_index("dp")
    particle_cache = jnp.concatenate([history, jnp.transpose(recent, (1, 0, 2))], axis=1)
    owners = ancestors.reshape(shards, part_dev)
    picked = jnp.max(jnp.where(owners // part_dev == own_index, owners % part_dev, 0), axis=1)
    outgoing = jnp.take(particle_cache, picked, axis=0)
    incoming = lax.all_to_all(outgoing, "dp", split_axis=0, concat_axis=0, tiled=True)
    own_ancestors = lax.dynamic_slice_in_dim(ancestors, own_index * part_dev, part_dev)
    return jnp.take(incoming, own_ancestors // part_dev, axis=0)[None]


def local(token_states, norm_gains, prompt_kv, history_kv, new_kv, ancestors):
    section_count = lax.axis_size("section")
    section_index = lax.axis_index("section")
    part_dev = history_kv.shape[1]
    steps = new_kv.shape[1]
    model_width = token_states.shape[2]
    half = KV_HEADS * HEAD_DIM
    gains = norm_gains
    prompt = prompt_kv[0]
    history = history_kv[0]
    recent = new_kv[0]
    cache = jnp.concatenate([history, jnp.transpose(recent, (1, 0, 2))], axis=1).reshape(
        -1, history.shape[2]
    )
    prompt_keys_t = prompt[:, :half].T
    cache_keys_t = cache[:, :half].T
    groups = 4
    group_rows = part_dev // groups
    grouped_tokens = token_states.reshape(steps, groups, group_rows, model_width)
    moments = steps * section_count + groups - 1

    def advance(moment, carry):
        arrived, outbuf = carry
        offset = moment - section_index
        step_raw = jnp.floor_divide(offset, section_count)
        group_raw = jnp.mod(offset, section_count)
        active = (offset >= 0) & (step_raw < steps) & (group_raw < groups)
        step_now = jnp.clip(step_raw, 0, steps - 1)
        group_now = jnp.clip(group_raw, 0, groups - 1)
        start = group_now * group_rows
        zero = jnp.zeros((), jnp.int32)
        scalars = jnp.stack(
            [step_now, group_now, (section_index == 0).astype(jnp.int32), (step_now > 0).astype(jnp.int32)]
        ).astype(jnp.int32)
        residual, mixed = stage(
            scalars, arrived, grouped_tokens, gains, prompt_keys_t, prompt, cache_keys_t, cache,
            history.shape[1],
        )
        previous = lax.dynamic_slice(outbuf, (step_now, start, zero), (1, group_rows, model_width))
        written = jnp.where(active, mixed[None], previous)
        outbuf = lax.dynamic_update_slice(outbuf, written, (step_now, start, zero))
        passed = passed_along(residual, "section", 1)
        return (passed, outbuf)

    start_carry = (
        jnp.zeros((group_rows, model_width), jnp.float32),
        jnp.zeros((steps, part_dev, model_width), jnp.bfloat16),
    )
    forked_kv = fork_cache(history, recent, ancestors, part_dev)
    _, outbuf = lax.fori_loop(0, moments, advance, start_carry)
    return (outbuf[None], forked_kv)


def solution(mesh):
    in_specs = (
        P(None, "dp", None),
        P("section", None),
        P("section", None, None),
        P("section", "dp", None, None),
        P("section", None, "dp", None),
        P(),
    )
    out_specs = (P("section", None, "dp", None), P("section", "dp", None, None))
    return jax.shard_map(local, mesh=mesh, in_specs=in_specs, out_specs=out_specs, check_vma=False)
```

```python
import jax
import jax.numpy as jnp
from jax import lax
from jax.experimental import pallas as pl
from jax.experimental.pallas import tpu as pltpu
from jax.sharding import PartitionSpec as P


HEADS = 64
KV_HEADS = 8
HEAD_DIM = 128


NEG_FILL = -1e30


def passed_along(block, axis, distance):
    devices = range(lax.axis_size(axis))
    route = [((i - distance) % len(devices), i) for i in devices]
    return lax.ppermute(block, axis, route)


def normalize(values):
    return values * lax.rsqrt(jnp.mean(values * values, axis=-1, keepdims=True) + 1e-05)


HEAD_BLOCK = 2
INTERPRET = False


def stage_kernel(rows, tokens, hist, head_block):
    score_scale = HEAD_DIM ** (-0.5)
    share = HEADS // KV_HEADS
    group_width = share * HEAD_DIM

    def kernel(
        sc_ref, arr_ref, tok_ref, gain_ref, pk_ref, pv_ref, ck_ref, cv_ref,
        res_ref, att_ref, hid_ref, q_ref,
    ):
        block = pl.program_id(0)

        @pl.when(block == 0)
        def _():
            arrived = arr_ref[...]
            carried = jnp.where(sc_ref[3] > 0, normalize(arrived), 0.0)
            hidden = jnp.where(sc_ref[2] > 0, tok_ref[...].astype(jnp.float32) + carried, arrived)
            queries = (normalize(hidden) * gain_ref[...]).astype(jnp.float32)
            for k in range(KV_HEADS):
                cols = slice(k * group_width, (k + 1) * group_width)
                hid_ref[k] = hidden[:, cols]
                q_ref[k] = queries[:, cols].reshape(rows * share, HEAD_DIM)

        step_now = sc_ref[0]
        width = ck_ref.shape[1]
        row_id = lax.broadcasted_iota(jnp.int32, (rows * share, width), 0)
        col_id = lax.broadcasted_iota(jnp.int32, (rows * share, width), 1)
        valid = (row_id // share == col_id // tokens) & (col_id % tokens < hist + 1 + step_now)
        for h in range(head_block):
            head = block * head_block + h
            cols = slice(h * HEAD_DIM, (h + 1) * HEAD_DIM)
            q = q_ref[head].astype(jnp.bfloat16)
            prompt_scores = (
                jnp.dot(q, pk_ref[cols, :], preferred_element_type=jnp.float32) * score_scale
            )
            cache_scores = (
                jnp.dot(q, ck_ref[cols, :], preferred_element_type=jnp.float32) * score_scale
            )
            cache_scores = jnp.where(valid, cache_scores, NEG_FILL)
            highest = jnp.maximum(
                jnp.max(prompt_scores, -1, keepdims=True), jnp.max(cache_scores, -1, keepdims=True)
            )
            prompt_exp = jnp.exp(prompt_scores - highest)
            cache_exp = jnp.exp(cache_scores - highest)
            denominator = jnp.sum(prompt_exp, -1, keepdims=True) + jnp.sum(
                cache_exp, -1, keepdims=True
            )
            mixed = jnp.dot(
                (prompt_exp / denominator).astype(jnp.bfloat16),
                pv_ref[:, cols],
                preferred_element_type=jnp.float32,
            )
            mixed = mixed + jnp.dot(
                (cache_exp / denominator).astype(jnp.bfloat16),
                cv_ref[:, cols],
                preferred_element_type=jnp.float32,
            )
            mixed = mixed.reshape(rows, group_width)
            out_cols = slice(h * group_width, (h + 1) * group_width)
            res_ref[:, out_cols] = hid_ref[head] + mixed
            att_ref[:, out_cols] = mixed.astype(jnp.bfloat16)

    return kernel


def stage(scalars, arrived, grouped_tokens, gains, prompt_keys_t, prompt, cache_keys_t, cache, hist_len):
    rows, model_width = arrived.shape
    share = HEADS // KV_HEADS
    tokens = cache.shape[0] // (grouped_tokens.shape[1] * rows)
    hb = HEAD_BLOCK
    nb = KV_HEADS // hb
    width = hb * HEAD_DIM
    grid_spec = pltpu.PrefetchScalarGridSpec(
        num_scalar_prefetch=1,
        grid=(nb,),
        in_specs=[
            pl.BlockSpec((rows, model_width), lambda i, sc: (0, 0)),
            pl.BlockSpec((None, None, rows, model_width), lambda i, sc: (sc[0], sc[1], 0, 0)),
            pl.BlockSpec((1, model_width), lambda i, sc: (0, 0)),
            pl.BlockSpec((width, prompt_keys_t.shape[1]), lambda i, sc: (i, 0)),
            pl.BlockSpec((prompt.shape[0], width), lambda i, sc: (0, i + nb)),
            pl.BlockSpec((width, rows * tokens), lambda i, sc: (i, sc[1])),
            pl.BlockSpec((rows * tokens, width), lambda i, sc: (sc[1], i + nb)),
        ],
        out_specs=[
            pl.BlockSpec((rows, hb * share * HEAD_DIM), lambda i, sc: (0, i)),
            pl.BlockSpec((rows, hb * share * HEAD_DIM), lambda i, sc: (0, i)),
        ],
        scratch_shapes=[
            pltpu.VMEM((KV_HEADS, rows, share * HEAD_DIM), jnp.float32),
            pltpu.VMEM((KV_HEADS, rows * share, HEAD_DIM), jnp.float32),
        ],
    )
    return pl.pallas_call(
        stage_kernel(rows, tokens, hist_len, hb),
        grid_spec=grid_spec,
        out_shape=[
            jax.ShapeDtypeStruct((rows, model_width), jnp.float32),
            jax.ShapeDtypeStruct((rows, model_width), jnp.bfloat16),
        ],
        compiler_params=pltpu.CompilerParams(dimension_semantics=("arbitrary",)),
        interpret=INTERPRET,
    )(scalars, arrived, grouped_tokens, gains, prompt_keys_t, prompt, cache_keys_t, cache)


def fork_cache(history, recent, ancestors, part_dev):
    shards = lax.axis_size("dp")
    own_index = lax.axis_index("dp")
    particle_cache = jnp.concatenate([history, jnp.transpose(recent, (1, 0, 2))], axis=1)
    owners = ancestors.reshape(shards, part_dev)
    picked = jnp.max(jnp.where(owners // part_dev == own_index, owners % part_dev, 0), axis=1)
    outgoing = jnp.take(particle_cache, picked, axis=0, mode="clip")
    incoming = lax.all_to_all(outgoing, "dp", split_axis=0, concat_axis=0, tiled=True)
    own_ancestors = lax.dynamic_slice_in_dim(ancestors, own_index * part_dev, part_dev)
    return jnp.take(incoming, own_ancestors // part_dev, axis=0, mode="clip")[None]


def local(token_states, norm_gains, prompt_kv, history_kv, new_kv, ancestors):
    section_count = lax.axis_size("section")
    section_index = lax.axis_index("section")
    part_dev = history_kv.shape[1]
    steps = new_kv.shape[1]
    model_width = token_states.shape[2]
    half = KV_HEADS * HEAD_DIM
    gains = norm_gains
    prompt = prompt_kv[0]
    history = history_kv[0]
    recent = new_kv[0]
    cache = jnp.concatenate([history, jnp.transpose(recent, (1, 0, 2))], axis=1).reshape(
        -1, history.shape[2]
    )
    prompt_keys_t = prompt[:, :half].T
    cache_keys_t = cache[:, :half].T
    groups = 4
    group_rows = part_dev // groups
    grouped_tokens = token_states.reshape(steps, groups, group_rows, model_width)
    moments = steps * section_count + groups - 1

    def timing(moment):
        offset = moment - section_index
        step_raw = jnp.floor_divide(offset, section_count)
        group_raw = jnp.mod(offset, section_count)
        active = (offset >= 0) & (step_raw < steps) & (group_raw < groups)
        step_now = jnp.clip(step_raw, 0, steps - 1)
        group_now = jnp.clip(group_raw, 0, groups - 1)
        scalars = jnp.stack(
            [step_now, group_now, (section_index == 0).astype(jnp.int32), (step_now > 0).astype(jnp.int32)]
        ).astype(jnp.int32)
        return active, step_now, group_now, scalars

    def advance(moment, carry):
        arrived, outbuf, scalars = carry
        active, step_now, group_now, _ = timing(moment)
        start = group_now * group_rows
        zero = jnp.zeros((), jnp.int32)
        residual, mixed = stage(
            scalars, arrived, grouped_tokens, gains, prompt_keys_t, prompt, cache_keys_t, cache,
            history.shape[1],
        )
        previous = lax.dynamic_slice(outbuf, (step_now, start, zero), (1, group_rows, model_width))
        written = jnp.where(active, mixed[None], previous)
        outbuf = lax.dynamic_update_slice(outbuf, written, (step_now, start, zero))
        passed = passed_along(residual, "section", 1)
        return (passed, outbuf, timing(moment + 1)[3])

    start_carry = (
        jnp.zeros((group_rows, model_width), jnp.float32),
        jnp.zeros((steps, part_dev, model_width), jnp.bfloat16),
        timing(jnp.zeros((), jnp.int32))[3],
    )
    forked_kv = fork_cache(history, recent, ancestors, part_dev)
    _, outbuf, _ = lax.fori_loop(0, moments, advance, start_carry)
    return (outbuf[None], forked_kv)


def solution(mesh):
    in_specs = (
        P(None, "dp", None),
        P("section", None),
        P("section", None, None),
        P("section", "dp", None, None),
        P("section", None, "dp", None),
        P(),
    )
    out_specs = (P("section", None, "dp", None), P("section", "dp", None, None))
    return jax.shard_map(local, mesh=mesh, in_specs=in_specs, out_specs=out_specs, check_vma=False)
```

```python
import jax
import jax.numpy as jnp
from jax import lax
from jax.experimental import pallas as pl
from jax.experimental.pallas import tpu as pltpu
from jax.sharding import PartitionSpec as P


HEADS = 64
KV_HEADS = 8
HEAD_DIM = 128


NEG_FILL = -1e30


def passed_along(block, axis, distance):
    devices = range(lax.axis_size(axis))
    route = [((i - distance) % len(devices), i) for i in devices]
    return lax.ppermute(block, axis, route)


def normalize(values):
    return values * lax.rsqrt(jnp.mean(values * values, axis=-1, keepdims=True) + 1e-05)


HEAD_BLOCK = 2
INTERPRET = False


def stage_kernel(rows, tokens, hist, head_block):
    score_scale = HEAD_DIM ** (-0.5)
    share = HEADS // KV_HEADS
    group_width = share * HEAD_DIM

    def kernel(
        sc_ref, arr_ref, tok_ref, gain_ref, pk_ref, pv_ref, ck_ref, cv_ref,
        res_ref, att_ref, hid_ref, q_ref,
    ):
        block = pl.program_id(0)

        @pl.when(block == 0)
        def _():
            arrived = arr_ref[...]
            carried = jnp.where(sc_ref[3] > 0, normalize(arrived), 0.0)
            hidden = jnp.where(sc_ref[2] > 0, tok_ref[...].astype(jnp.float32) + carried, arrived)
            queries = (normalize(hidden) * gain_ref[...]).astype(jnp.float32)
            for k in range(KV_HEADS):
                cols = slice(k * group_width, (k + 1) * group_width)
                hid_ref[k] = hidden[:, cols]
                q_ref[k] = queries[:, cols].reshape(rows * share, HEAD_DIM)

        step_now = sc_ref[0]
        width = ck_ref.shape[1]
        row_id = lax.broadcasted_iota(jnp.int32, (rows * share, width), 0)
        col_id = lax.broadcasted_iota(jnp.int32, (rows * share, width), 1)
        valid = (row_id // share == col_id // tokens) & (col_id % tokens < hist + 1 + step_now)
        for h in range(head_block):
            head = block * head_block + h
            cols = slice(h * HEAD_DIM, (h + 1) * HEAD_DIM)
            q = q_ref[head].astype(jnp.bfloat16)
            dims = (((1,), (1,)), ((), ()))
            prompt_scores = (
                lax.dot_general(q, pk_ref[:, cols], dims, preferred_element_type=jnp.float32)
                * score_scale
            )
            cache_scores = (
                lax.dot_general(q, ck_ref[:, cols], dims, preferred_element_type=jnp.float32)
                * score_scale
            )
            cache_scores = jnp.where(valid, cache_scores, NEG_FILL)
            highest = jnp.maximum(
                jnp.max(prompt_scores, -1, keepdims=True), jnp.max(cache_scores, -1, keepdims=True)
            )
            prompt_exp = jnp.exp(prompt_scores - highest)
            cache_exp = jnp.exp(cache_scores - highest)
            denominator = jnp.sum(prompt_exp, -1, keepdims=True) + jnp.sum(
                cache_exp, -1, keepdims=True
            )
            mixed = jnp.dot(
                (prompt_exp / denominator).astype(jnp.bfloat16),
                pv_ref[:, cols],
                preferred_element_type=jnp.float32,
            )
            mixed = mixed + jnp.dot(
                (cache_exp / denominator).astype(jnp.bfloat16),
                cv_ref[:, cols],
                preferred_element_type=jnp.float32,
            )
            mixed = mixed.reshape(rows, group_width)
            out_cols = slice(h * group_width, (h + 1) * group_width)
            res_ref[:, out_cols] = hid_ref[head] + mixed
            att_ref[:, out_cols] = mixed.astype(jnp.bfloat16)

    return kernel


def stage(scalars, arrived, grouped_tokens, gains, prompt, cache, hist_len):
    rows, model_width = arrived.shape
    share = HEADS // KV_HEADS
    tokens = cache.shape[0] // (grouped_tokens.shape[1] * rows)
    hb = HEAD_BLOCK
    nb = KV_HEADS // hb
    width = hb * HEAD_DIM
    grid_spec = pltpu.PrefetchScalarGridSpec(
        num_scalar_prefetch=1,
        grid=(nb,),
        in_specs=[
            pl.BlockSpec((rows, model_width), lambda i, sc: (0, 0)),
            pl.BlockSpec((None, None, rows, model_width), lambda i, sc: (sc[0], sc[1], 0, 0)),
            pl.BlockSpec((1, model_width), lambda i, sc: (0, 0)),
            pl.BlockSpec((prompt.shape[0], width), lambda i, sc: (0, i)),
            pl.BlockSpec((prompt.shape[0], width), lambda i, sc: (0, i + nb)),
            pl.BlockSpec((rows * tokens, width), lambda i, sc: (sc[1], i)),
            pl.BlockSpec((rows * tokens, width), lambda i, sc: (sc[1], i + nb)),
        ],
        out_specs=[
            pl.BlockSpec((rows, hb * share * HEAD_DIM), lambda i, sc: (0, i)),
            pl.BlockSpec((rows, hb * share * HEAD_DIM), lambda i, sc: (0, i)),
        ],
        scratch_shapes=[
            pltpu.VMEM((KV_HEADS, rows, share * HEAD_DIM), jnp.float32),
            pltpu.VMEM((KV_HEADS, rows * share, HEAD_DIM), jnp.float32),
        ],
    )
    return pl.pallas_call(
        stage_kernel(rows, tokens, hist_len, hb),
        grid_spec=grid_spec,
        out_shape=[
            jax.ShapeDtypeStruct((rows, model_width), jnp.float32),
            jax.ShapeDtypeStruct((rows, model_width), jnp.bfloat16),
        ],
        compiler_params=pltpu.CompilerParams(dimension_semantics=("arbitrary",)),
        interpret=INTERPRET,
    )(scalars, arrived, grouped_tokens, gains, prompt, prompt, cache, cache)


def fork_cache(history, recent, ancestors, part_dev):
    shards = lax.axis_size("dp")
    own_index = lax.axis_index("dp")
    particle_cache = jnp.concatenate([history, jnp.transpose(recent, (1, 0, 2))], axis=1)
    owners = ancestors.reshape(shards, part_dev)
    picked = jnp.max(jnp.where(owners // part_dev == own_index, owners % part_dev, 0), axis=1)
    outgoing = jnp.take(particle_cache, picked, axis=0, mode="clip")
    incoming = lax.all_to_all(outgoing, "dp", split_axis=0, concat_axis=0, tiled=True)
    own_ancestors = lax.dynamic_slice_in_dim(ancestors, own_index * part_dev, part_dev)
    return jnp.take(incoming, own_ancestors // part_dev, axis=0, mode="clip")[None]


def local(token_states, norm_gains, prompt_kv, history_kv, new_kv, ancestors):
    section_count = lax.axis_size("section")
    section_index = lax.axis_index("section")
    part_dev = history_kv.shape[1]
    steps = new_kv.shape[1]
    model_width = token_states.shape[2]
    gains = norm_gains
    prompt = prompt_kv[0]
    history = history_kv[0]
    recent = new_kv[0]
    cache = jnp.concatenate([history, jnp.transpose(recent, (1, 0, 2))], axis=1).reshape(
        -1, history.shape[2]
    )
    groups = 2
    group_rows = part_dev // groups
    grouped_tokens = token_states.reshape(steps, groups, group_rows, model_width)
    moments = steps * section_count + groups - 1

    def timing(moment):
        offset = moment - section_index
        step_raw = jnp.floor_divide(offset, section_count)
        group_raw = jnp.mod(offset, section_count)
        active = (offset >= 0) & (step_raw < steps) & (group_raw < groups)
        step_now = jnp.clip(step_raw, 0, steps - 1)
        group_now = jnp.clip(group_raw, 0, groups - 1)
        scalars = jnp.stack(
            [step_now, group_now, (section_index == 0).astype(jnp.int32), (step_now > 0).astype(jnp.int32)]
        ).astype(jnp.int32)
        return active, step_now, group_now, scalars

    def advance(moment, carry):
        arrived, outbuf, scalars = carry
        active, step_now, group_now, _ = timing(moment)
        start = group_now * group_rows
        zero = jnp.zeros((), jnp.int32)
        residual, mixed = stage(
            scalars, arrived, grouped_tokens, gains, prompt, cache,
            history.shape[1],
        )
        previous = lax.dynamic_slice(outbuf, (step_now, start, zero), (1, group_rows, model_width))
        written = jnp.where(active, mixed[None], previous)
        outbuf = lax.dynamic_update_slice(outbuf, written, (step_now, start, zero))
        passed = passed_along(residual, "section", 1)
        return (passed, outbuf, timing(moment + 1)[3])

    start_carry = (
        jnp.zeros((group_rows, model_width), jnp.float32),
        jnp.zeros((steps, part_dev, model_width), jnp.bfloat16),
        timing(jnp.zeros((), jnp.int32))[3],
    )
    forked_kv = fork_cache(history, recent, ancestors, part_dev)
    _, outbuf, _ = lax.fori_loop(0, moments, advance, start_carry)
    return (outbuf[None], forked_kv)


def solution(mesh):
    in_specs = (
        P(None, "dp", None),
        P("section", None),
        P("section", None, None),
        P("section", "dp", None, None),
        P("section", None, "dp", None),
        P(),
    )
    out_specs = (P("section", None, "dp", None), P("section", "dp", None, None))
    return jax.shard_map(local, mesh=mesh, in_specs=in_specs, out_specs=out_specs, check_vma=False)
```

```python
import jax
import jax.numpy as jnp
from jax import lax
from jax.experimental import pallas as pl
from jax.experimental.pallas import tpu as pltpu
from jax.sharding import PartitionSpec as P


HEADS = 64
KV_HEADS = 8
HEAD_DIM = 128


NEG_FILL = -1e30


def passed_along(block, axis, distance):
    devices = range(lax.axis_size(axis))
    route = [((i - distance) % len(devices), i) for i in devices]
    return lax.ppermute(block, axis, route)


def normalize(values):
    return values * lax.rsqrt(jnp.mean(values * values, axis=-1, keepdims=True) + 1e-05)


HEAD_BLOCK = 2
INTERPRET = False


def stage_kernel(rows, tokens, hist, head_block):
    score_scale = HEAD_DIM ** (-0.5)
    share = HEADS // KV_HEADS
    group_width = share * HEAD_DIM

    def kernel(
        sc_ref, arr_ref, tok_ref, gain_ref, pk_ref, pv_ref, ck_ref, cv_ref,
        res_ref, att_ref, hid_ref, q_ref,
    ):
        block = pl.program_id(0)

        @pl.when(block == 0)
        def _():
            arrived = arr_ref[...]
            carried = jnp.where(sc_ref[3] > 0, normalize(arrived), 0.0)
            hidden = jnp.where(sc_ref[2] > 0, tok_ref[...].astype(jnp.float32) + carried, arrived)
            queries = (normalize(hidden) * gain_ref[...]).astype(jnp.float32)
            for k in range(KV_HEADS):
                cols = slice(k * group_width, (k + 1) * group_width)
                hid_ref[k] = hidden[:, cols]
                q_ref[k] = queries[:, cols].reshape(rows * share, HEAD_DIM)

        step_now = sc_ref[0]
        width = ck_ref.shape[0]
        row_id = lax.broadcasted_iota(jnp.int32, (rows * share, width), 0)
        col_id = lax.broadcasted_iota(jnp.int32, (rows * share, width), 1)
        valid = (row_id // share == col_id // tokens) & (col_id % tokens < hist + 1 + step_now)
        for h in range(head_block):
            head = block * head_block + h
            cols = slice(h * HEAD_DIM, (h + 1) * HEAD_DIM)
            q = q_ref[head].astype(jnp.bfloat16)
            dims = (((1,), (1,)), ((), ()))
            prompt_scores = (
                lax.dot_general(q, pk_ref[:, cols], dims, preferred_element_type=jnp.float32)
                * score_scale
            )
            cache_scores = (
                lax.dot_general(q, ck_ref[:, cols], dims, preferred_element_type=jnp.float32)
                * score_scale
            )
            cache_scores = jnp.where(valid, cache_scores, NEG_FILL)
            highest = jnp.maximum(
                jnp.max(prompt_scores, -1, keepdims=True), jnp.max(cache_scores, -1, keepdims=True)
            )
            prompt_exp = jnp.exp(prompt_scores - highest)
            cache_exp = jnp.exp(cache_scores - highest)
            denominator = jnp.sum(prompt_exp, -1, keepdims=True) + jnp.sum(
                cache_exp, -1, keepdims=True
            )
            inverse = 1.0 / denominator
            mixed = jnp.dot(
                (prompt_exp * inverse).astype(jnp.bfloat16),
                pv_ref[:, cols],
                preferred_element_type=jnp.float32,
            )
            mixed = mixed + jnp.dot(
                (cache_exp * inverse).astype(jnp.bfloat16),
                cv_ref[:, cols],
                preferred_element_type=jnp.float32,
            )
            mixed = mixed.reshape(rows, group_width)
            out_cols = slice(h * group_width, (h + 1) * group_width)
            res_ref[:, out_cols] = hid_ref[head] + mixed
            att_ref[:, out_cols] = mixed.astype(jnp.bfloat16)

    return kernel


def stage(scalars, arrived, grouped_tokens, gains, prompt, cache, hist_len):
    rows, model_width = arrived.shape
    share = HEADS // KV_HEADS
    tokens = cache.shape[0] // (grouped_tokens.shape[1] * rows)
    hb = HEAD_BLOCK
    nb = KV_HEADS // hb
    width = hb * HEAD_DIM
    grid_spec = pltpu.PrefetchScalarGridSpec(
        num_scalar_prefetch=1,
        grid=(nb,),
        in_specs=[
            pl.BlockSpec((rows, model_width), lambda i, sc: (0, 0)),
            pl.BlockSpec((None, None, rows, model_width), lambda i, sc: (sc[0], sc[1], 0, 0)),
            pl.BlockSpec((1, model_width), lambda i, sc: (0, 0)),
            pl.BlockSpec((prompt.shape[0], width), lambda i, sc: (0, i)),
            pl.BlockSpec((prompt.shape[0], width), lambda i, sc: (0, i + nb)),
            pl.BlockSpec((rows * tokens, width), lambda i, sc: (sc[1], i)),
            pl.BlockSpec((rows * tokens, width), lambda i, sc: (sc[1], i + nb)),
        ],
        out_specs=[
            pl.BlockSpec((rows, hb * share * HEAD_DIM), lambda i, sc: (0, i)),
            pl.BlockSpec((rows, hb * share * HEAD_DIM), lambda i, sc: (0, i)),
        ],
        scratch_shapes=[
            pltpu.VMEM((KV_HEADS, rows, share * HEAD_DIM), jnp.float32),
            pltpu.VMEM((KV_HEADS, rows * share, HEAD_DIM), jnp.float32),
        ],
    )
    return pl.pallas_call(
        stage_kernel(rows, tokens, hist_len, hb),
        grid_spec=grid_spec,
        out_shape=[
            jax.ShapeDtypeStruct((rows, model_width), jnp.float32),
            jax.ShapeDtypeStruct((rows, model_width), jnp.bfloat16),
        ],
        compiler_params=pltpu.CompilerParams(dimension_semantics=("arbitrary",)),
        interpret=INTERPRET,
    )(scalars, arrived, grouped_tokens, gains, prompt, prompt, cache, cache)


def fork_cache(history, recent, ancestors, part_dev):
    shards = lax.axis_size("dp")
    own_index = lax.axis_index("dp")
    particle_cache = jnp.concatenate([history, jnp.transpose(recent, (1, 0, 2))], axis=1)
    owners = ancestors.reshape(shards, part_dev)
    picked = jnp.max(jnp.where(owners // part_dev == own_index, owners % part_dev, 0), axis=1)
    outgoing = jnp.take(particle_cache, picked, axis=0, mode="clip")
    incoming = lax.all_to_all(outgoing, "dp", split_axis=0, concat_axis=0, tiled=True)
    own_ancestors = lax.dynamic_slice_in_dim(ancestors, own_index * part_dev, part_dev)
    return jnp.take(incoming, own_ancestors // part_dev, axis=0, mode="clip")[None]


def local(token_states, norm_gains, prompt_kv, history_kv, new_kv, ancestors):
    section_count = lax.axis_size("section")
    section_index = lax.axis_index("section")
    part_dev = history_kv.shape[1]
    steps = new_kv.shape[1]
    model_width = token_states.shape[2]
    gains = norm_gains
    prompt = prompt_kv[0]
    history = history_kv[0]
    recent = new_kv[0]
    cache = jnp.concatenate([history, jnp.transpose(recent, (1, 0, 2))], axis=1).reshape(
        -1, history.shape[2]
    )
    groups = 4
    group_rows = part_dev // groups
    grouped_tokens = token_states.reshape(steps, groups, group_rows, model_width)
    moments = steps * section_count + groups - 1

    def timing(moment):
        offset = moment - section_index
        step_raw = jnp.floor_divide(offset, section_count)
        group_raw = jnp.mod(offset, section_count)
        active = (offset >= 0) & (step_raw < steps) & (group_raw < groups)
        step_now = jnp.clip(step_raw, 0, steps - 1)
        group_now = jnp.clip(group_raw, 0, groups - 1)
        scalars = jnp.stack(
            [step_now, group_now, (section_index == 0).astype(jnp.int32), (step_now > 0).astype(jnp.int32)]
        ).astype(jnp.int32)
        return active, step_now, group_now, scalars

    def advance(moment, carry):
        arrived, outbuf, scalars = carry
        active, step_now, group_now, _ = timing(moment)
        start = group_now * group_rows
        zero = jnp.zeros((), jnp.int32)
        residual, mixed = stage(
            scalars, arrived, grouped_tokens, gains, prompt, cache,
            history.shape[1],
        )
        previous = lax.dynamic_slice(outbuf, (step_now, start, zero), (1, group_rows, model_width))
        written = jnp.where(active, mixed[None], previous)
        outbuf = lax.dynamic_update_slice(outbuf, written, (step_now, start, zero))
        passed = passed_along(residual, "section", 1)
        return (passed, outbuf, timing(moment + 1)[3])

    start_carry = (
        jnp.zeros((group_rows, model_width), jnp.float32),
        jnp.zeros((steps, part_dev, model_width), jnp.bfloat16),
        timing(jnp.zeros((), jnp.int32))[3],
    )
    forked_kv = fork_cache(history, recent, ancestors, part_dev)
    _, outbuf, _ = lax.fori_loop(0, moments, advance, start_carry)
    return (outbuf[None], forked_kv)


def solution(mesh):
    in_specs = (
        P(None, "dp", None),
        P("section", None),
        P("section", None, None),
        P("section", "dp", None, None),
        P("section", None, "dp", None),
        P(),
    )
    out_specs = (P("section", None, "dp", None), P("section", "dp", None, None))
    return jax.shard_map(local, mesh=mesh, in_specs=in_specs, out_specs=out_specs, check_vma=False)
```

```python
import jax
import jax.numpy as jnp
from jax import lax
from jax.experimental import pallas as pl
from jax.experimental.pallas import tpu as pltpu
from jax.sharding import PartitionSpec as P


HEADS = 64
KV_HEADS = 8
HEAD_DIM = 128


NEG_FILL = -1e30


def passed_along(block, axis, distance):
    devices = range(lax.axis_size(axis))
    route = [((i - distance) % len(devices), i) for i in devices]
    return lax.ppermute(block, axis, route)


def normalize(values):
    return values * lax.rsqrt(jnp.mean(values * values, axis=-1, keepdims=True) + 1e-05)


HEAD_BLOCK = 4
INTERPRET = False


def stage_kernel(rows, tokens, hist, head_block):
    score_scale = HEAD_DIM ** (-0.5)
    share = HEADS // KV_HEADS
    group_width = share * HEAD_DIM

    def kernel(
        sc_ref, arr_ref, tok_ref, gain_ref, pk_ref, pv_ref, ck_ref, cv_ref,
        res_ref, att_ref, hid_ref, q_ref,
    ):
        block = pl.program_id(0)

        @pl.when(block == 0)
        def _():
            arrived = arr_ref[...]
            carried = jnp.where(sc_ref[3] > 0, normalize(arrived), 0.0)
            hidden = jnp.where(sc_ref[2] > 0, tok_ref[...].astype(jnp.float32) + carried, arrived)
            queries = (normalize(hidden) * gain_ref[...]).astype(jnp.float32)
            for k in range(KV_HEADS):
                cols = slice(k * group_width, (k + 1) * group_width)
                hid_ref[k] = hidden[:, cols]
                q_ref[k] = queries[:, cols].reshape(rows * share, HEAD_DIM)

        step_now = sc_ref[0]
        width = ck_ref.shape[0]
        row_id = lax.broadcasted_iota(jnp.int32, (rows * share, width), 0)
        col_id = lax.broadcasted_iota(jnp.int32, (rows * share, width), 1)
        valid = (row_id // share == col_id // tokens) & (col_id % tokens < hist + 1 + step_now)
        dims = (((1,), (1,)), ((), ()))

        def scores(h):
            head = block * head_block + h
            cols = slice(h * HEAD_DIM, (h + 1) * HEAD_DIM)
            q = q_ref[head].astype(jnp.bfloat16)
            prompt_scores = (
                lax.dot_general(q, pk_ref[:, cols], dims, preferred_element_type=jnp.float32)
                * score_scale
            )
            cache_scores = (
                lax.dot_general(q, ck_ref[:, cols], dims, preferred_element_type=jnp.float32)
                * score_scale
            )
            return prompt_scores, jnp.where(valid, cache_scores, NEG_FILL)

        pending = scores(0)
        for h in range(head_block):
            head = block * head_block + h
            cols = slice(h * HEAD_DIM, (h + 1) * HEAD_DIM)
            prompt_scores, cache_scores = pending
            if h + 1 < head_block:
                pending = scores(h + 1)
            highest = jnp.maximum(
                jnp.max(prompt_scores, -1, keepdims=True), jnp.max(cache_scores, -1, keepdims=True)
            )
            prompt_exp = jnp.exp(prompt_scores - highest)
            cache_exp = jnp.exp(cache_scores - highest)
            denominator = jnp.sum(prompt_exp, -1, keepdims=True) + jnp.sum(
                cache_exp, -1, keepdims=True
            )
            inverse = 1.0 / denominator
            mixed = jnp.dot(
                (prompt_exp * inverse).astype(jnp.bfloat16),
                pv_ref[:, cols],
                preferred_element_type=jnp.float32,
            )
            mixed = mixed + jnp.dot(
                (cache_exp * inverse).astype(jnp.bfloat16),
                cv_ref[:, cols],
                preferred_element_type=jnp.float32,
            )
            mixed = mixed.reshape(rows, group_width)
            out_cols = slice(h * group_width, (h + 1) * group_width)
            res_ref[:, out_cols] = hid_ref[head] + mixed
            att_ref[:, out_cols] = mixed.astype(jnp.bfloat16)

    return kernel


def stage(scalars, arrived, grouped_tokens, gains, prompt, cache, hist_len):
    rows, model_width = arrived.shape
    share = HEADS // KV_HEADS
    tokens = cache.shape[0] // (grouped_tokens.shape[1] * rows)
    hb = HEAD_BLOCK
    nb = KV_HEADS // hb
    width = hb * HEAD_DIM
    grid_spec = pltpu.PrefetchScalarGridSpec(
        num_scalar_prefetch=1,
        grid=(nb,),
        in_specs=[
            pl.BlockSpec((rows, model_width), lambda i, sc: (0, 0)),
            pl.BlockSpec((None, None, rows, model_width), lambda i, sc: (sc[0], sc[1], 0, 0)),
            pl.BlockSpec((1, model_width), lambda i, sc: (0, 0)),
            pl.BlockSpec((prompt.shape[0], width), lambda i, sc: (0, i)),
            pl.BlockSpec((prompt.shape[0], width), lambda i, sc: (0, i + nb)),
            pl.BlockSpec((rows * tokens, width), lambda i, sc: (sc[1], i)),
            pl.BlockSpec((rows * tokens, width), lambda i, sc: (sc[1], i + nb)),
        ],
        out_specs=[
            pl.BlockSpec((rows, hb * share * HEAD_DIM), lambda i, sc: (0, i)),
            pl.BlockSpec((rows, hb * share * HEAD_DIM), lambda i, sc: (0, i)),
        ],
        scratch_shapes=[
            pltpu.VMEM((KV_HEADS, rows, share * HEAD_DIM), jnp.float32),
            pltpu.VMEM((KV_HEADS, rows * share, HEAD_DIM), jnp.float32),
        ],
    )
    return pl.pallas_call(
        stage_kernel(rows, tokens, hist_len, hb),
        grid_spec=grid_spec,
        out_shape=[
            jax.ShapeDtypeStruct((rows, model_width), jnp.float32),
            jax.ShapeDtypeStruct((rows, model_width), jnp.bfloat16),
        ],
        compiler_params=pltpu.CompilerParams(dimension_semantics=("arbitrary",)),
        interpret=INTERPRET,
    )(scalars, arrived, grouped_tokens, gains, prompt, prompt, cache, cache)


def fork_cache(history, recent, ancestors, part_dev):
    shards = lax.axis_size("dp")
    own_index = lax.axis_index("dp")
    particle_cache = jnp.concatenate([history, jnp.transpose(recent, (1, 0, 2))], axis=1)
    owners = ancestors.reshape(shards, part_dev)
    picked = jnp.max(jnp.where(owners // part_dev == own_index, owners % part_dev, 0), axis=1)
    outgoing = jnp.take(particle_cache, picked, axis=0, mode="clip")
    incoming = lax.all_to_all(outgoing, "dp", split_axis=0, concat_axis=0, tiled=True)
    own_ancestors = lax.dynamic_slice_in_dim(ancestors, own_index * part_dev, part_dev)
    return jnp.take(incoming, own_ancestors // part_dev, axis=0, mode="clip")[None]


def local(token_states, norm_gains, prompt_kv, history_kv, new_kv, ancestors):
    section_count = lax.axis_size("section")
    section_index = lax.axis_index("section")
    part_dev = history_kv.shape[1]
    steps = new_kv.shape[1]
    model_width = token_states.shape[2]
    gains = norm_gains
    prompt = prompt_kv[0]
    history = history_kv[0]
    recent = new_kv[0]
    cache = jnp.concatenate([history, jnp.transpose(recent, (1, 0, 2))], axis=1).reshape(
        -1, history.shape[2]
    )
    groups = 4
    group_rows = part_dev // groups
    grouped_tokens = token_states.reshape(steps, groups, group_rows, model_width)
    moments = steps * section_count + groups - 1

    def timing(moment):
        offset = moment - section_index
        step_raw = jnp.floor_divide(offset, section_count)
        group_raw = jnp.mod(offset, section_count)
        active = (offset >= 0) & (step_raw < steps) & (group_raw < groups)
        step_now = jnp.clip(step_raw, 0, steps - 1)
        group_now = jnp.clip(group_raw, 0, groups - 1)
        scalars = jnp.stack(
            [step_now, group_now, (section_index == 0).astype(jnp.int32), (step_now > 0).astype(jnp.int32)]
        ).astype(jnp.int32)
        return active, step_now, group_now, scalars

    def advance(moment, carry):
        arrived, outbuf, scalars = carry
        active, step_now, group_now, _ = timing(moment)
        start = group_now * group_rows
        zero = jnp.zeros((), jnp.int32)
        residual, mixed = stage(
            scalars, arrived, grouped_tokens, gains, prompt, cache,
            history.shape[1],
        )
        previous = lax.dynamic_slice(outbuf, (step_now, start, zero), (1, group_rows, model_width))
        written = jnp.where(active, mixed[None], previous)
        outbuf = lax.dynamic_update_slice(outbuf, written, (step_now, start, zero))
        passed = passed_along(residual, "section", 1)
        return (passed, outbuf, timing(moment + 1)[3])

    start_carry = (
        jnp.zeros((group_rows, model_width), jnp.float32),
        jnp.zeros((steps, part_dev, model_width), jnp.bfloat16),
        timing(jnp.zeros((), jnp.int32))[3],
    )
    forked_kv = fork_cache(history, recent, ancestors, part_dev)
    _, outbuf, _ = lax.fori_loop(0, moments, advance, start_carry)
    return (outbuf[None], forked_kv)


def solution(mesh):
    in_specs = (
        P(None, "dp", None),
        P("section", None),
        P("section", None, None),
        P("section", "dp", None, None),
        P("section", None, "dp", None),
        P(),
    )
    out_specs = (P("section", None, "dp", None), P("section", "dp", None, None))
    return jax.shard_map(local, mesh=mesh, in_specs=in_specs, out_specs=out_specs, check_vma=False)
```

```python
import jax
import jax.numpy as jnp
from jax import lax
from jax.experimental import pallas as pl
from jax.experimental.pallas import tpu as pltpu
from jax.sharding import PartitionSpec as P


HEADS = 64
KV_HEADS = 8
HEAD_DIM = 128


NEG_FILL = -1e30


def passed_along(block, axis, distance):
    devices = range(lax.axis_size(axis))
    route = [((i - distance) % len(devices), i) for i in devices]
    return lax.ppermute(block, axis, route)


def normalize(values):
    return values * lax.rsqrt(jnp.mean(values * values, axis=-1, keepdims=True) + 1e-05)


HEAD_BLOCK = 4
LOOKAHEAD = 4
INTERPRET = False


def stage_kernel(rows, tokens, hist, head_block):
    score_scale = HEAD_DIM ** (-0.5)
    share = HEADS // KV_HEADS
    group_width = share * HEAD_DIM

    def kernel(
        sc_ref, arr_ref, tok_ref, gain_ref, pk_ref, pv_ref, ck_ref, cv_ref,
        res_ref, att_ref, hid_ref, q_ref,
    ):
        block = pl.program_id(0)

        @pl.when(block == 0)
        def _():
            arrived = arr_ref[...]
            carried = jnp.where(sc_ref[3] > 0, normalize(arrived), 0.0)
            hidden = jnp.where(sc_ref[2] > 0, tok_ref[...].astype(jnp.float32) + carried, arrived)
            queries = (normalize(hidden) * gain_ref[...]).astype(jnp.float32)
            for k in range(KV_HEADS):
                cols = slice(k * group_width, (k + 1) * group_width)
                hid_ref[k] = hidden[:, cols]
                q_ref[k] = queries[:, cols].reshape(rows * share, HEAD_DIM)

        step_now = sc_ref[0]
        width = ck_ref.shape[0]
        row_id = lax.broadcasted_iota(jnp.int32, (rows * share, width), 0)
        col_id = lax.broadcasted_iota(jnp.int32, (rows * share, width), 1)
        valid = (row_id // share == col_id // tokens) & (col_id % tokens < hist + 1 + step_now)
        dims = (((1,), (1,)), ((), ()))

        def scores(h):
            head = block * head_block + h
            cols = slice(h * HEAD_DIM, (h + 1) * HEAD_DIM)
            q = q_ref[head].astype(jnp.bfloat16)
            prompt_scores = (
                lax.dot_general(q, pk_ref[:, cols], dims, preferred_element_type=jnp.float32)
                * score_scale
            )
            cache_scores = (
                lax.dot_general(q, ck_ref[:, cols], dims, preferred_element_type=jnp.float32)
                * score_scale
            )
            return prompt_scores, jnp.where(valid, cache_scores, NEG_FILL)

        pending = {h: scores(h) for h in range(min(LOOKAHEAD, head_block))}
        for h in range(head_block):
            head = block * head_block + h
            cols = slice(h * HEAD_DIM, (h + 1) * HEAD_DIM)
            prompt_scores, cache_scores = pending.pop(h)
            if h + LOOKAHEAD < head_block:
                pending[h + LOOKAHEAD] = scores(h + LOOKAHEAD)
            highest = jnp.maximum(
                jnp.max(prompt_scores, -1, keepdims=True), jnp.max(cache_scores, -1, keepdims=True)
            )
            prompt_exp = jnp.exp(prompt_scores - highest)
            cache_exp = jnp.exp(cache_scores - highest)
            denominator = jnp.sum(prompt_exp, -1, keepdims=True) + jnp.sum(
                cache_exp, -1, keepdims=True
            )
            inverse = 1.0 / denominator
            mixed = jnp.dot(
                (prompt_exp * inverse).astype(jnp.bfloat16),
                pv_ref[:, cols],
                preferred_element_type=jnp.float32,
            )
            mixed = mixed + jnp.dot(
                (cache_exp * inverse).astype(jnp.bfloat16),
                cv_ref[:, cols],
                preferred_element_type=jnp.float32,
            )
            mixed = mixed.reshape(rows, group_width)
            out_cols = slice(h * group_width, (h + 1) * group_width)
            res_ref[:, out_cols] = hid_ref[head] + mixed
            att_ref[:, out_cols] = mixed.astype(jnp.bfloat16)

    return kernel


def stage(scalars, arrived, grouped_tokens, gains, prompt, cache, hist_len):
    rows, model_width = arrived.shape
    share = HEADS // KV_HEADS
    tokens = cache.shape[0] // (grouped_tokens.shape[1] * rows)
    hb = HEAD_BLOCK
    nb = KV_HEADS // hb
    width = hb * HEAD_DIM
    grid_spec = pltpu.PrefetchScalarGridSpec(
        num_scalar_prefetch=1,
        grid=(nb,),
        in_specs=[
            pl.BlockSpec((rows, model_width), lambda i, sc: (0, 0)),
            pl.BlockSpec((None, None, rows, model_width), lambda i, sc: (sc[0], sc[1], 0, 0)),
            pl.BlockSpec((1, model_width), lambda i, sc: (0, 0)),
            pl.BlockSpec((prompt.shape[0], width), lambda i, sc: (0, i)),
            pl.BlockSpec((prompt.shape[0], width), lambda i, sc: (0, i + nb)),
            pl.BlockSpec((rows * tokens, width), lambda i, sc: (sc[1], i)),
            pl.BlockSpec((rows * tokens, width), lambda i, sc: (sc[1], i + nb)),
        ],
        out_specs=[
            pl.BlockSpec((rows, hb * share * HEAD_DIM), lambda i, sc: (0, i)),
            pl.BlockSpec((rows, hb * share * HEAD_DIM), lambda i, sc: (0, i)),
        ],
        scratch_shapes=[
            pltpu.VMEM((KV_HEADS, rows, share * HEAD_DIM), jnp.float32),
            pltpu.VMEM((KV_HEADS, rows * share, HEAD_DIM), jnp.float32),
        ],
    )
    return pl.pallas_call(
        stage_kernel(rows, tokens, hist_len, hb),
        grid_spec=grid_spec,
        out_shape=[
            jax.ShapeDtypeStruct((rows, model_width), jnp.float32),
            jax.ShapeDtypeStruct((rows, model_width), jnp.bfloat16),
        ],
        compiler_params=pltpu.CompilerParams(dimension_semantics=("arbitrary",)),
        interpret=INTERPRET,
    )(scalars, arrived, grouped_tokens, gains, prompt, prompt, cache, cache)


def fork_cache(history, recent, ancestors, part_dev):
    shards = lax.axis_size("dp")
    own_index = lax.axis_index("dp")
    particle_cache = jnp.concatenate([history, jnp.transpose(recent, (1, 0, 2))], axis=1)
    owners = ancestors.reshape(shards, part_dev)
    picked = jnp.max(jnp.where(owners // part_dev == own_index, owners % part_dev, 0), axis=1)
    outgoing = jnp.take(particle_cache, picked, axis=0, mode="clip")
    incoming = lax.all_to_all(outgoing, "dp", split_axis=0, concat_axis=0, tiled=True)
    own_ancestors = lax.dynamic_slice_in_dim(ancestors, own_index * part_dev, part_dev)
    picks = (own_ancestors // part_dev).astype(jnp.int32)

    def copy_rows(idx_ref, src_hbm, dst_hbm, sems):
        copies = [
            pltpu.make_async_copy(src_hbm.at[idx_ref[j]], dst_hbm.at[j], sems.at[j])
            for j in range(part_dev)
        ]
        for c in copies:
            c.start()
        for c in copies:
            c.wait()

    chosen = pl.pallas_call(
        copy_rows,
        grid_spec=pltpu.PrefetchScalarGridSpec(
            num_scalar_prefetch=1,
            grid=(1,),
            in_specs=[pl.BlockSpec(memory_space=pl.ANY)],
            out_specs=pl.BlockSpec(memory_space=pl.ANY),
            scratch_shapes=[pltpu.SemaphoreType.DMA((part_dev,))],
        ),
        out_shape=jax.ShapeDtypeStruct((part_dev,) + incoming.shape[1:], incoming.dtype),
        interpret=INTERPRET,
    )(picks, incoming)
    return chosen[None]


def local(token_states, norm_gains, prompt_kv, history_kv, new_kv, ancestors):
    section_count = lax.axis_size("section")
    section_index = lax.axis_index("section")
    part_dev = history_kv.shape[1]
    steps = new_kv.shape[1]
    model_width = token_states.shape[2]
    gains = norm_gains
    prompt = prompt_kv[0]
    history = history_kv[0]
    recent = new_kv[0]
    cache = jnp.concatenate([history, jnp.transpose(recent, (1, 0, 2))], axis=1).reshape(
        -1, history.shape[2]
    )
    groups = 4
    group_rows = part_dev // groups
    grouped_tokens = token_states.reshape(steps, groups, group_rows, model_width)
    moments = steps * section_count + groups - 1

    def timing(moment):
        offset = moment - section_index
        step_raw = jnp.floor_divide(offset, section_count)
        group_raw = jnp.mod(offset, section_count)
        active = (offset >= 0) & (step_raw < steps) & (group_raw < groups)
        step_now = jnp.clip(step_raw, 0, steps - 1)
        group_now = jnp.clip(group_raw, 0, groups - 1)
        scalars = jnp.stack(
            [step_now, group_now, (section_index == 0).astype(jnp.int32), (step_now > 0).astype(jnp.int32)]
        ).astype(jnp.int32)
        return active, step_now, group_now, scalars

    def advance(moment, carry):
        arrived, outbuf, scalars = carry
        active, step_now, group_now, _ = timing(moment)
        start = group_now * group_rows
        zero = jnp.zeros((), jnp.int32)
        residual, mixed = stage(
            scalars, arrived, grouped_tokens, gains, prompt, cache,
            history.shape[1],
        )
        previous = lax.dynamic_slice(outbuf, (step_now, start, zero), (1, group_rows, model_width))
        written = jnp.where(active, mixed[None], previous)
        outbuf = lax.dynamic_update_slice(outbuf, written, (step_now, start, zero))
        passed = passed_along(residual, "section", 1)
        return (passed, outbuf, timing(moment + 1)[3])

    start_carry = (
        jnp.zeros((group_rows, model_width), jnp.float32),
        jnp.zeros((steps, part_dev, model_width), jnp.bfloat16),
        timing(jnp.zeros((), jnp.int32))[3],
    )
    first_carry = advance(jnp.zeros((), jnp.int32), start_carry)
    forked_kv = fork_cache(history, recent, ancestors, part_dev)
    _, outbuf, _ = lax.fori_loop(1, moments, advance, first_carry)
    return (outbuf[None], forked_kv)


def solution(mesh):
    in_specs = (
        P(None, "dp", None),
        P("section", None),
        P("section", None, None),
        P("section", "dp", None, None),
        P("section", None, "dp", None),
        P(),
    )
    out_specs = (P("section", None, "dp", None), P("section", "dp", None, None))
    return jax.shard_map(local, mesh=mesh, in_specs=in_specs, out_specs=out_specs, check_vma=False)
```

```python
import jax
import jax.numpy as jnp
from jax import lax
from jax.experimental import pallas as pl
from jax.experimental.pallas import tpu as pltpu
from jax.sharding import PartitionSpec as P


HEADS = 64
KV_HEADS = 8
HEAD_DIM = 128


NEG_FILL = -1e30


def passed_along(block, axis, distance):
    devices = range(lax.axis_size(axis))
    route = [((i - distance) % len(devices), i) for i in devices]
    return lax.ppermute(block, axis, route)


def normalize(values):
    return values * lax.rsqrt(jnp.mean(values * values, axis=-1, keepdims=True) + 1e-05)


HEAD_BLOCK = 4
LOOKAHEAD = 4
INTERPRET = False


def stage_kernel(rows, tokens, hist, head_block):
    score_scale = HEAD_DIM ** (-0.5)
    share = HEADS // KV_HEADS
    group_width = share * HEAD_DIM

    def kernel(
        sc_ref, arr_ref, tok_ref, gain_ref, pk_ref, pv_ref, ck_ref, cv_ref,
        res_ref, att_ref, hid_ref, q_ref,
    ):
        block = pl.program_id(0)

        @pl.when(block == 0)
        def _():
            arrived = arr_ref[...]
            carried = jnp.where(sc_ref[3] > 0, normalize(arrived), 0.0)
            hidden = jnp.where(sc_ref[2] > 0, tok_ref[...].astype(jnp.float32) + carried, arrived)
            queries = (normalize(hidden) * gain_ref[...]).astype(jnp.float32)
            for k in range(KV_HEADS):
                cols = slice(k * group_width, (k + 1) * group_width)
                hid_ref[k] = hidden[:, cols]
                q_ref[k] = queries[:, cols].reshape(rows * share, HEAD_DIM)

        step_now = sc_ref[0]
        width = ck_ref.shape[0]
        row_id = lax.broadcasted_iota(jnp.int32, (rows * share, width), 0)
        col_id = lax.broadcasted_iota(jnp.int32, (rows * share, width), 1)
        valid = (row_id // share == col_id // tokens) & (col_id % tokens < hist + 1 + step_now)
        dims = (((1,), (1,)), ((), ()))

        def scores(h):
            head = block * head_block + h
            cols = slice(h * HEAD_DIM, (h + 1) * HEAD_DIM)
            q = q_ref[head].astype(jnp.bfloat16)
            prompt_scores = (
                lax.dot_general(q, pk_ref[:, cols], dims, preferred_element_type=jnp.float32)
                * score_scale
            )
            cache_scores = (
                lax.dot_general(q, ck_ref[:, cols], dims, preferred_element_type=jnp.float32)
                * score_scale
            )
            return prompt_scores, jnp.where(valid, cache_scores, NEG_FILL)

        pending = {h: scores(h) for h in range(min(LOOKAHEAD, head_block))}
        for h in range(head_block):
            head = block * head_block + h
            cols = slice(h * HEAD_DIM, (h + 1) * HEAD_DIM)
            prompt_scores, cache_scores = pending.pop(h)
            if h + LOOKAHEAD < head_block:
                pending[h + LOOKAHEAD] = scores(h + LOOKAHEAD)
            highest = jnp.maximum(
                jnp.max(prompt_scores, -1, keepdims=True), jnp.max(cache_scores, -1, keepdims=True)
            )
            prompt_exp = jnp.exp(prompt_scores - highest)
            cache_exp = jnp.exp(cache_scores - highest)
            denominator = jnp.sum(prompt_exp, -1, keepdims=True) + jnp.sum(
                cache_exp, -1, keepdims=True
            )
            inverse = 1.0 / denominator
            mixed = jnp.dot(
                (prompt_exp * inverse).astype(jnp.bfloat16),
                pv_ref[:, cols],
                preferred_element_type=jnp.float32,
            )
            mixed = mixed + jnp.dot(
                (cache_exp * inverse).astype(jnp.bfloat16),
                cv_ref[:, cols],
                preferred_element_type=jnp.float32,
            )
            mixed = mixed.reshape(rows, group_width)
            out_cols = slice(h * group_width, (h + 1) * group_width)
            res_ref[:, out_cols] = hid_ref[head] + mixed
            att_ref[:, out_cols] = mixed.astype(jnp.bfloat16)

    return kernel


def stage(scalars, arrived, grouped_tokens, gains, prompt, cache, hist_len):
    rows, model_width = arrived.shape
    share = HEADS // KV_HEADS
    tokens = cache.shape[0] // (grouped_tokens.shape[1] * rows)
    hb = HEAD_BLOCK
    nb = KV_HEADS // hb
    width = hb * HEAD_DIM
    grid_spec = pltpu.PrefetchScalarGridSpec(
        num_scalar_prefetch=1,
        grid=(nb,),
        in_specs=[
            pl.BlockSpec((rows, model_width), lambda i, sc: (0, 0)),
            pl.BlockSpec((None, None, rows, model_width), lambda i, sc: (sc[0], sc[1], 0, 0)),
            pl.BlockSpec((1, model_width), lambda i, sc: (0, 0)),
            pl.BlockSpec((prompt.shape[0], width), lambda i, sc: (0, i)),
            pl.BlockSpec((prompt.shape[0], width), lambda i, sc: (0, i + nb)),
            pl.BlockSpec((rows * tokens, width), lambda i, sc: (sc[1], i)),
            pl.BlockSpec((rows * tokens, width), lambda i, sc: (sc[1], i + nb)),
        ],
        out_specs=[
            pl.BlockSpec((rows, hb * share * HEAD_DIM), lambda i, sc: (0, i)),
            pl.BlockSpec((rows, hb * share * HEAD_DIM), lambda i, sc: (0, i)),
        ],
        scratch_shapes=[
            pltpu.VMEM((KV_HEADS, rows, share * HEAD_DIM), jnp.float32),
            pltpu.VMEM((KV_HEADS, rows * share, HEAD_DIM), jnp.float32),
        ],
    )
    return pl.pallas_call(
        stage_kernel(rows, tokens, hist_len, hb),
        grid_spec=grid_spec,
        out_shape=[
            jax.ShapeDtypeStruct((rows, model_width), jnp.float32),
            jax.ShapeDtypeStruct((rows, model_width), jnp.bfloat16),
        ],
        compiler_params=pltpu.CompilerParams(dimension_semantics=("arbitrary",)),
        interpret=INTERPRET,
    )(scalars, arrived, grouped_tokens, gains, prompt, prompt, cache, cache)


def fork_cache(history, recent, ancestors, part_dev):
    shards = lax.axis_size("dp")
    own_index = lax.axis_index("dp")
    particle_cache = jnp.concatenate([history, jnp.transpose(recent, (1, 0, 2))], axis=1)
    owners = ancestors.reshape(shards, part_dev)
    picked = jnp.max(jnp.where(owners // part_dev == own_index, owners % part_dev, 0), axis=1)
    outgoing = jnp.take(particle_cache, picked, axis=0, mode="clip")
    incoming = lax.all_to_all(outgoing, "dp", split_axis=0, concat_axis=0, tiled=True)
    own_ancestors = lax.dynamic_slice_in_dim(ancestors, own_index * part_dev, part_dev)
    return jnp.take(incoming, own_ancestors // part_dev, axis=0, mode="clip")[None]


def local(token_states, norm_gains, prompt_kv, history_kv, new_kv, ancestors):
    section_count = lax.axis_size("section")
    section_index = lax.axis_index("section")
    part_dev = history_kv.shape[1]
    steps = new_kv.shape[1]
    model_width = token_states.shape[2]
    gains = norm_gains
    prompt = prompt_kv[0]
    history = history_kv[0]
    recent = new_kv[0]
    cache = jnp.concatenate([history, jnp.transpose(recent, (1, 0, 2))], axis=1).reshape(
        -1, history.shape[2]
    )
    groups = 4
    group_rows = part_dev // groups
    grouped_tokens = token_states.reshape(steps, groups, group_rows, model_width)
    moments = steps * section_count + groups - 1

    def timing(moment):
        offset = moment - section_index
        step_raw = jnp.floor_divide(offset, section_count)
        group_raw = jnp.mod(offset, section_count)
        active = (offset >= 0) & (step_raw < steps) & (group_raw < groups)
        step_now = jnp.clip(step_raw, 0, steps - 1)
        group_now = jnp.clip(group_raw, 0, groups - 1)
        scalars = jnp.stack(
            [step_now, group_now, (section_index == 0).astype(jnp.int32), (step_now > 0).astype(jnp.int32)]
        ).astype(jnp.int32)
        return active, step_now, group_now, scalars

    def advance(moment, carry):
        arrived, outbuf, scalars = carry
        active, step_now, group_now, _ = timing(moment)
        start = group_now * group_rows
        zero = jnp.zeros((), jnp.int32)
        residual, mixed = stage(
            scalars, arrived, grouped_tokens, gains, prompt, cache,
            history.shape[1],
        )
        previous = lax.dynamic_slice(outbuf, (step_now, start, zero), (1, group_rows, model_width))
        written = jnp.where(active, mixed[None], previous)
        outbuf = lax.dynamic_update_slice(outbuf, written, (step_now, start, zero))
        passed = passed_along(residual, "section", 1)
        return (passed, outbuf, timing(moment + 1)[3])

    start_carry = (
        jnp.zeros((group_rows, model_width), jnp.float32),
        jnp.zeros((steps, part_dev, model_width), jnp.bfloat16),
        timing(jnp.zeros((), jnp.int32))[3],
    )
    first_carry = advance(jnp.zeros((), jnp.int32), start_carry)
    first_carry = advance(jnp.ones((), jnp.int32), first_carry)
    forked_kv = fork_cache(history, recent, ancestors, part_dev)
    _, outbuf, _ = lax.fori_loop(2, moments, advance, first_carry)
    return (outbuf[None], forked_kv)


def solution(mesh):
    in_specs = (
        P(None, "dp", None),
        P("section", None),
        P("section", None, None),
        P("section", "dp", None, None),
        P("section", None, "dp", None),
        P(),
    )
    out_specs = (P("section", None, "dp", None), P("section", "dp", None, None))
    return jax.shard_map(local, mesh=mesh, in_specs=in_specs, out_specs=out_specs, check_vma=False)
```
